256 devices in a mesh: ctx: 32 (over y, z), rep: 8 (over x, core).
Axes of the slice: x: 4, y: 4, z: 8, core: 2. Of those that a mesh axis runs over, the one named last changes fastest.
Arguments:
- queries: bfloat16 [32768, 4096], P(('rep', 'ctx')), parts along dimension 0, may hold values from -6 to 6
- key_rows: bfloat16 [32768, 4096], P(('rep', 'ctx')), parts along dimension 0, may hold values from -6 to 6
- value_rows: bfloat16 [32768, 4096], P(('rep', 'ctx')), parts along dimension 0, may hold values from -8 to 8
- doc_blocks: int32 [24], P('rep'), parts along dimension 0, may hold values from 1 to 16, 32 in all
- phm_mix: float32 [4, 4, 4], replicated, may hold values from -4 to 4
- phm_blocks: bfloat16 [4096, 1280], P('ctx'), may hold values from -0.09375 to 0.09375
Outputs:
- projected: bfloat16 [32768, 5120], P(('rep', 'ctx')), parts along dimension 0
The draws below stay inside these ranges and needn't reach their ends.
There are 8 independent parts, one for each index of `rep`. The reference program is written for one: setup_inputs(seed, part) draws one part's arguments, and reference() takes and returns one part's arrays. A program takes and returns all parts, laid end to end along the dimension named above; an argument that names none is the same for every part. Nothing has to cross between parts.
Inputs may be any that keep to these rules, and one draw needn't show every extreme that they name: `doc_blocks`: entries sum to 32; the largest entry is exactly 16.
All inputs are finite; a program needn't handle non-finite values.
Results may differ from the reference program's by a relative error of at most 0.006.
Values may be sent and summed in bfloat16 or wider, within the bound.
No kernel may reach another device: no remote copies, remote signals or barrier semaphores. Data moves between devices by JAX's collectives and lax.ppermute only.
A program may use at most 64 MiB of HBM per device.

```python
import math
import jax
import jax.numpy as jnp
import numpy as np
from jax import lax

HEAD_DIM = 128
PHM_N = 4
UNIT = 128
HEADS = 32
SEQ = 4096
DOC_MOST = 2048
DOCS = 3
ROWS_PHM = 1024
COLS_PHM = 1280


def drawn_pair(key):
    base = jax.random.fold_in(key, 17)
    key_first, key_second = jax.random.split(base, 2)
    width = HEADS * HEAD_DIM
    first = 1.4 * jax.random.truncated_normal(key_first, -4.2, 4.2, (SEQ, width), jnp.float32)
    second = 1.4 * jax.random.truncated_normal(key_second, -4.2, 4.2, (SEQ, width), jnp.float32)
    return (first, second)


def draw_queries(key, part):
    return drawn_pair(key)[0].astype(jnp.bfloat16)


def draw_key_rows(key, part):
    return drawn_pair(key)[1].astype(jnp.bfloat16)


def level_of(stream_key, dims, shards, least, largest):
    def one(dim, shards_of):
        steps = jax.random.uniform(jax.random.fold_in(jax.random.fold_in(stream_key, 6), dim), (shards_of,), jnp.float32, least / len(shards), largest / len(shards))
        return jnp.repeat(jnp.exp(steps), dims[dim] // shards_of).reshape((-1,) + (1,) * (len(dims) - dim - 1))

    loudness = one(*shards[0])
    for cut in shards[1:]:
        loudness = loudness * one(*cut)
    return loudness


def split_up(count, total, most, lean):
    portions = [(1 << 20) // math.isqrt(rank ** lean) + 1 for rank in range(2, count + 1)]
    surplus, counts = total - most - (count - 1), [1] * (count - 1)
    while surplus > 0:
        candidates = [i for i in range(count - 1) if counts[i] < most]
        whole, budget = sum([portions[i] for i in candidates]), surplus
        for i in candidates:
            extra = min(most - counts[i], max(1, budget * portions[i] // whole), surplus)
            counts[i] = counts[i] + extra
            surplus = surplus - extra
    return np.array([most] + counts)


def ragged(stream_key, count, total, reach, slope):
    if count == 2:
        one = jax.random.randint(stream_key, (), max(1, total - reach), min(reach, total - 1) + 1)
        return jnp.stack([one, total - one])
    sizes = jnp.asarray(split_up(count, total, reach, slope), jnp.int32)
    pairs = (count - 1) // 2
    giver, receiver = sizes[1:1 + 2 * pairs:2], sizes[2:2 + 2 * pairs:2]
    room = jnp.minimum(giver - 1, reach - receiver)
    shifted = jax.random.randint(jax.random.fold_in(stream_key, 1), (pairs,), 0, 1 << 20) % (room + 1)
    sizes = sizes.at[1:1 + 2 * pairs:2].set(giver - shifted).at[2:2 + 2 * pairs:2].set(receiver + shifted)
    return sizes[jax.random.permutation(jax.random.fold_in(stream_key, 2), count)]


def bell_draw(stream_key, dims, spread, bound, shards=(), kind=jnp.bfloat16):
    values = spread * jax.random.normal(stream_key, dims, jnp.float32)
    if shards:
        values = values * level_of(stream_key, dims, shards, -0.22, 0.18)
    return jnp.clip(values, -bound, bound).astype(kind)


def setup_inputs(seed: int = 0, part: int = 0) -> dict:
    seeds = jax.random.split(jax.random.key(seed), 7)
    part_keys = jax.random.split(jax.random.fold_in(seeds[6], part), 7)
    return {
        "queries": draw_queries(jax.random.fold_in(jax.random.fold_in(seeds[6], part), 71), part),
        "key_rows": draw_key_rows(jax.random.fold_in(jax.random.fold_in(seeds[6], part), 71), part),
        "value_rows": bell_draw(part_keys[2], (SEQ, HEADS * HEAD_DIM), 2.0, 8.0, ((0, 32),)),
        "doc_blocks": ragged(part_keys[3], DOCS, SEQ // UNIT, DOC_MOST // UNIT, 2).astype(jnp.int32),
        "phm_mix": bell_draw(seeds[4], (PHM_N, PHM_N, PHM_N), 1.0, 4.0, (), jnp.float32),
        "phm_blocks": bell_draw(seeds[5], (PHM_N * ROWS_PHM, COLS_PHM), (PHM_N * ROWS_PHM) ** -0.5, 0.09375, ((0, 32),)),
    }


def reference(queries, key_rows, value_rows, doc_blocks, phm_mix, phm_blocks):
    seq_len = queries.shape[0]
    ends = jnp.cumsum(doc_blocks.astype(jnp.int32) * UNIT).astype(jnp.int32)
    positions = jnp.arange(seq_len, dtype=jnp.int32)
    doc_ids = lax.optimization_barrier(jnp.sum((positions[:, None] >= ends[None, :]).astype(jnp.int32), axis=1))
    allowed = (positions[None, :] <= positions[:, None]) & (doc_ids[None, :] == doc_ids[:, None])
    scale = 1.0 / math.sqrt(HEAD_DIM)
    heads = queries.shape[1] // HEAD_DIM
    q_heads = queries.reshape(seq_len, heads, HEAD_DIM).transpose(1, 0, 2)
    k_heads = key_rows.reshape(seq_len, heads, HEAD_DIM).transpose(1, 0, 2)
    v_heads = value_rows.reshape(seq_len, heads, HEAD_DIM).transpose(1, 0, 2)

    def one_head(operands):
        q_one, k_one, v_one = operands
        scores = jnp.dot(q_one, k_one.T, preferred_element_type=jnp.float32) * scale
        scores = jnp.where(allowed, scores, -jnp.inf)
        row_max = lax.optimization_barrier(jnp.max(scores, axis=1, keepdims=True))
        expd = jnp.where(allowed, jnp.exp(scores - row_max), 0.0)
        totals = lax.optimization_barrier(jnp.sum(expd, axis=1, keepdims=True))
        probs = expd.astype(jnp.bfloat16)
        attended = jnp.dot(probs, v_one, preferred_element_type=jnp.float32) / totals
        return attended.astype(jnp.bfloat16)
    attended = lax.map(one_head, (q_heads, k_heads, v_heads))
    attended = attended.transpose(1, 0, 2).reshape(seq_len, heads * HEAD_DIM)
    rows_phm = heads * HEAD_DIM // PHM_N
    pieces = attended.reshape(seq_len, PHM_N, rows_phm).astype(jnp.float32)
    mixed = jnp.einsum('iab,tar->tbir', phm_mix.astype(jnp.float32), pieces, precision=lax.Precision.HIGHEST)
    mixed = mixed.astype(jnp.bfloat16).reshape(seq_len, PHM_N, PHM_N * rows_phm)
    result = jnp.einsum('tbk,kc->tbc', mixed.astype(jnp.float32), phm_blocks.astype(jnp.float32))
    return result.reshape(seq_len, PHM_N * phm_blocks.shape[1]).astype(jnp.bfloat16)
```

```python
import functools
import math

import jax
import jax.numpy as jnp
from jax import lax
from jax.experimental import pallas as pl
from jax.experimental.pallas import tpu as pltpu
from jax.sharding import PartitionSpec as P

HEAD_DIM = 128
PHM_N = 4
UNIT = 128
BQ = 256
BK = 256


def flash_kernel(ends_ref, q_ref, k_ref, v_ref, o_ref):
    i = pl.program_id(0)
    e0 = ends_ref[0]
    e1 = ends_ref[1]
    scale = 1.0 / math.sqrt(HEAD_DIM)

    def doc_start(t):
        return jnp.where(t >= e1, e1, jnp.where(t >= e0, e0, 0))

    q_lo = i * BQ
    j_lo = doc_start(q_lo) // BK
    j_hi = (q_lo + BQ - 1) // BK
    q = q_ref[...]
    q_pos = q_lo + lax.broadcasted_iota(jnp.int32, (BQ, 1), 0)
    q_start = doc_start(q_pos)

    def body(j, carry):
        m, l, acc = carry
        base = pl.multiple_of(j * BK, BK)
        k = k_ref[pl.ds(base, BK), :]
        v = v_ref[pl.ds(base, BK), :]
        s = lax.dot_general(
            q, k, (((1,), (1,)), ((), ())), preferred_element_type=jnp.float32
        ) * scale
        k_pos = base + lax.broadcasted_iota(jnp.int32, (1, BK), 1)
        mask = (k_pos <= q_pos) & (k_pos >= q_start)
        s = jnp.where(mask, s, -1e30)
        m_new = jnp.maximum(m, jnp.max(s, axis=1, keepdims=True))
        p = jnp.where(mask, jnp.exp(s - m_new), 0.0)
        alpha = jnp.exp(m - m_new)
        l = alpha * l + jnp.sum(p, axis=1, keepdims=True)
        acc = alpha * acc + jnp.dot(
            p.astype(jnp.bfloat16), v, preferred_element_type=jnp.float32
        )
        return m_new, l, acc

    carry = (
        jnp.full((BQ, 1), -1e30, jnp.float32),
        jnp.zeros((BQ, 1), jnp.float32),
        jnp.zeros((BQ, HEAD_DIM), jnp.float32),
    )
    m, l, acc = lax.fori_loop(j_lo, j_hi + 1, body, carry)
    o_ref[...] = (acc / l).astype(o_ref.dtype)


def attend(q, k, v, ends):
    seq = q.shape[0]
    full = pl.BlockSpec((seq, HEAD_DIM), lambda i, e: (0, 0))
    return pl.pallas_call(
        flash_kernel,
        grid_spec=pltpu.PrefetchScalarGridSpec(
            num_scalar_prefetch=1,
            grid=(seq // BQ,),
            in_specs=[
                pl.BlockSpec((BQ, HEAD_DIM), lambda i, e: (i, 0)),
                full,
                full,
            ],
            out_specs=pl.BlockSpec((BQ, HEAD_DIM), lambda i, e: (i, 0)),
        ),
        out_shape=jax.ShapeDtypeStruct((seq, HEAD_DIM), jnp.bfloat16),
    )(ends, q, k, v)


def body(queries, key_rows, value_rows, doc_blocks, phm_mix, phm_blocks):
    tok_rows = queries.shape[0]
    heads = queries.shape[1] // HEAD_DIM
    stacked = jnp.stack([queries, key_rows, value_rows]).reshape(3, tok_rows, heads, HEAD_DIM)
    gathered = lax.all_to_all(stacked, "ctx", split_axis=2, concat_axis=1, tiled=True)
    seq_len = gathered.shape[1]
    q_all = gathered[0].reshape(seq_len, HEAD_DIM)
    k_all = gathered[1].reshape(seq_len, HEAD_DIM)
    v_all = gathered[2].reshape(seq_len, HEAD_DIM)
    ends = jnp.cumsum(doc_blocks.astype(jnp.int32) * UNIT).astype(jnp.int32)
    attended = attend(q_all, k_all, v_all, ends).reshape(seq_len, 1, HEAD_DIM)
    returned = lax.all_to_all(attended, "ctx", split_axis=0, concat_axis=1, tiled=True)
    rows_phm = heads * HEAD_DIM // PHM_N
    pieces = returned.reshape(tok_rows, PHM_N, rows_phm).astype(jnp.float32)
    mixed = jnp.einsum("iab,tar->tbir", phm_mix, pieces, precision=lax.Precision.HIGHEST)
    mixed = mixed.astype(jnp.bfloat16).reshape(tok_rows, PHM_N, PHM_N * rows_phm)
    cols_phm = phm_blocks.shape[1]
    output = jnp.einsum(
        "tbk,kc->tbc",
        mixed,
        lax.all_gather(phm_blocks, "ctx", axis=0, tiled=True),
        preferred_element_type=jnp.float32,
    )
    return output.reshape(tok_rows, PHM_N * cols_phm).astype(jnp.bfloat16)


def solution(mesh):
    placed = (
        P(("rep", "ctx"), None),
        P(("rep", "ctx"), None),
        P(("rep", "ctx"), None),
        P("rep"),
        P(),
        P("ctx", None),
    )
    return jax.shard_map(
        body, mesh=mesh, in_specs=placed, out_specs=P(("rep", "ctx"), None), check_vma=False
    )
```

```python
import functools
import math

import jax
import jax.numpy as jnp
from jax import lax
from jax.experimental import pallas as pl
from jax.experimental.pallas import tpu as pltpu
from jax.sharding import PartitionSpec as P

HEAD_DIM = 128
PHM_N = 4
UNIT = 128
BQ = 256
BK = 256


def flash_kernel(ends_ref, q_ref, k_ref, v_ref, o_ref):
    i = pl.program_id(0)
    e0 = ends_ref[0]
    e1 = ends_ref[1]
    scale = 1.0 / math.sqrt(HEAD_DIM)

    def doc_start(t):
        return jnp.where(t >= e1, e1, jnp.where(t >= e0, e0, 0))

    q_lo = i * BQ
    j_lo = doc_start(q_lo) // BK
    j_hi = (q_lo + BQ - 1) // BK
    q = q_ref[...]
    q_pos = q_lo + lax.broadcasted_iota(jnp.int32, (BQ, 1), 0)
    q_start = doc_start(q_pos)

    def body(j, carry):
        m, l, acc = carry
        base = pl.multiple_of(j * BK, BK)
        k = k_ref[pl.ds(base, BK), :]
        v = v_ref[pl.ds(base, BK), :]
        s = lax.dot_general(
            q, k, (((1,), (1,)), ((), ())), preferred_element_type=jnp.float32
        ) * scale
        k_pos = base + lax.broadcasted_iota(jnp.int32, (1, BK), 1)
        mask = (k_pos <= q_pos) & (k_pos >= q_start)
        s = jnp.where(mask, s, -1e30)
        m_new = jnp.maximum(m, jnp.max(s, axis=1, keepdims=True))
        p = jnp.where(mask, jnp.exp(s - m_new), 0.0)
        alpha = jnp.exp(m - m_new)
        l = alpha * l + jnp.sum(p, axis=1, keepdims=True)
        acc = alpha * acc + jnp.dot(
            p.astype(jnp.bfloat16), v, preferred_element_type=jnp.float32
        )
        return m_new, l, acc

    carry = (
        jnp.full((BQ, 1), -1e30, jnp.float32),
        jnp.zeros((BQ, 1), jnp.float32),
        jnp.zeros((BQ, HEAD_DIM), jnp.float32),
    )
    m, l, acc = lax.fori_loop(j_lo, j_hi + 1, body, carry)
    o_ref[...] = (acc / l).astype(o_ref.dtype)


def attend(q, k, v, ends):
    seq = q.shape[0]
    full = pl.BlockSpec((seq, HEAD_DIM), lambda i, e: (0, 0))
    return pl.pallas_call(
        flash_kernel,
        grid_spec=pltpu.PrefetchScalarGridSpec(
            num_scalar_prefetch=1,
            grid=(seq // BQ,),
            in_specs=[
                pl.BlockSpec((BQ, HEAD_DIM), lambda i, e: (i, 0)),
                full,
                full,
            ],
            out_specs=pl.BlockSpec((BQ, HEAD_DIM), lambda i, e: (i, 0)),
        ),
        out_shape=jax.ShapeDtypeStruct((seq, HEAD_DIM), jnp.bfloat16),
    )(ends, q, k, v)


def proj_kernel(mix_ref, att_ref, w_ref, o_ref, acc_ref):
    i = pl.program_id(0)
    rows = w_ref.shape[0]
    cols = w_ref.shape[1]

    @pl.when(i == 0)
    def _():
        acc_ref[...] = jnp.zeros_like(acc_ref)

    pieces = [att_ref[:, a * rows:(a + 1) * rows].astype(jnp.float32) for a in range(PHM_N)]
    w = w_ref[...]
    for b in range(PHM_N):
        mixed = pieces[0] * mix_ref[(i * PHM_N + 0) * PHM_N + b]
        for a in range(1, PHM_N):
            mixed = mixed + pieces[a] * mix_ref[(i * PHM_N + a) * PHM_N + b]
        acc_ref[b] += jnp.dot(mixed.astype(jnp.bfloat16), w, preferred_element_type=jnp.float32)

    @pl.when(i == PHM_N - 1)
    def _():
        for b in range(PHM_N):
            o_ref[:, b * cols:(b + 1) * cols] = acc_ref[b].astype(o_ref.dtype)


def project(att, mix, w):
    tok, width = att.shape
    rows = width // PHM_N
    cols = w.shape[1]
    return pl.pallas_call(
        proj_kernel,
        grid=(PHM_N,),
        in_specs=[
            pl.BlockSpec(memory_space=pltpu.SMEM),
            pl.BlockSpec((tok, width), lambda i: (0, 0)),
            pl.BlockSpec((rows, cols), lambda i: (i, 0)),
        ],
        out_specs=pl.BlockSpec((tok, PHM_N * cols), lambda i: (0, 0)),
        out_shape=jax.ShapeDtypeStruct((tok, PHM_N * cols), jnp.bfloat16),
        scratch_shapes=[pltpu.VMEM((PHM_N, tok, cols), jnp.float32)],
    )(mix.reshape(-1), att, w)


def gather_factors(phm_blocks):
    shard, cols = phm_blocks.shape
    n_x = lax.axis_size("x")
    n_core = lax.axis_size("core")
    piece = shard // (n_x * n_core)
    rho = lax.axis_index("x") * n_core + lax.axis_index("core")
    mine = lax.dynamic_slice_in_dim(phm_blocks, rho * piece, piece, 0)
    over_ctx = lax.all_gather(mine, "ctx", axis=0)
    over_x = lax.all_gather(over_ctx, "x", axis=0)
    over_core = lax.all_gather(over_x, "core", axis=0)
    return over_core.transpose(2, 1, 0, 3, 4).reshape(-1, cols)


def body(queries, key_rows, value_rows, doc_blocks, phm_mix, phm_blocks):
    tok_rows = queries.shape[0]
    heads = queries.shape[1] // HEAD_DIM
    factors = gather_factors(phm_blocks)
    stacked = jnp.stack([queries, key_rows, value_rows]).reshape(3, tok_rows, heads, HEAD_DIM)
    gathered = lax.all_to_all(stacked, "ctx", split_axis=2, concat_axis=1, tiled=True)
    seq_len = gathered.shape[1]
    q_all = gathered[0].reshape(seq_len, HEAD_DIM)
    k_all = gathered[1].reshape(seq_len, HEAD_DIM)
    v_all = gathered[2].reshape(seq_len, HEAD_DIM)
    ends = jnp.cumsum(doc_blocks.astype(jnp.int32) * UNIT).astype(jnp.int32)
    attended = attend(q_all, k_all, v_all, ends).reshape(seq_len, 1, HEAD_DIM)
    returned = lax.all_to_all(attended, "ctx", split_axis=0, concat_axis=1, tiled=True)
    return project(returned.reshape(tok_rows, heads * HEAD_DIM), phm_mix, factors)


def solution(mesh):
    rep_at = mesh.axis_names.index("rep")
    shape = list(mesh.devices.shape)
    shape[rep_at:rep_at + 1] = [shape[rep_at] // 2, 2]
    names = list(mesh.axis_names)
    names[rep_at:rep_at + 1] = ["x", "core"]
    split = jax.sharding.Mesh(mesh.devices.reshape(shape), tuple(names))
    rows = P(("x", "core", "ctx"), None)
    placed = (rows, rows, rows, P(("x", "core")), P(), P("ctx", None))
    return jax.shard_map(body, mesh=split, in_specs=placed, out_specs=rows, check_vma=False)
```

```python
import functools
import math

import jax
import jax.numpy as jnp
from jax import lax
from jax.experimental import pallas as pl
from jax.experimental.pallas import tpu as pltpu
from jax.sharding import PartitionSpec as P

HEAD_DIM = 128
PHM_N = 4
UNIT = 128
BQ = 256
BK = 256


def flash_kernel(ends_ref, q_ref, k_ref, v_ref, o_ref):
    i = pl.program_id(0)
    e0 = ends_ref[0]
    e1 = ends_ref[1]
    scale = 1.0 / math.sqrt(HEAD_DIM)

    def doc_start(t):
        return jnp.where(t >= e1, e1, jnp.where(t >= e0, e0, 0))

    q_lo = i * BQ
    j_lo = doc_start(q_lo) // BK
    j_hi = (q_lo + BQ - 1) // BK
    q = q_ref[...]
    q_pos = q_lo + lax.broadcasted_iota(jnp.int32, (BQ, 1), 0)
    q_start = doc_start(q_pos)

    def body(j, carry):
        m, l, acc = carry
        base = pl.multiple_of(j * BK, BK)
        k = k_ref[pl.ds(base, BK), :]
        v = v_ref[pl.ds(base, BK), :]
        s = lax.dot_general(
            q, k, (((1,), (1,)), ((), ())), preferred_element_type=jnp.float32
        ) * scale
        k_pos = base + lax.broadcasted_iota(jnp.int32, (1, BK), 1)
        mask = (k_pos <= q_pos) & (k_pos >= q_start)
        s = jnp.where(mask, s, -1e30)
        m_new = jnp.maximum(m, jnp.max(s, axis=1, keepdims=True))
        p = jnp.where(mask, jnp.exp(s - m_new), 0.0)
        alpha = jnp.exp(m - m_new)
        l = alpha * l + jnp.sum(p, axis=1, keepdims=True)
        acc = alpha * acc + jnp.dot(
            p.astype(jnp.bfloat16), v, preferred_element_type=jnp.float32
        )
        return m_new, l, acc

    carry = (
        jnp.full((BQ, 1), -1e30, jnp.float32),
        jnp.zeros((BQ, 1), jnp.float32),
        jnp.zeros((BQ, HEAD_DIM), jnp.float32),
    )
    m, l, acc = lax.fori_loop(j_lo, j_hi + 1, body, carry)
    o_ref[...] = (acc / l).astype(o_ref.dtype)

def attend(qkv, ends):
    seq = qkv.shape[1]

    def full(which):
        return pl.BlockSpec((None, seq, HEAD_DIM), lambda i, e: (which, 0, 0))

    return pl.pallas_call(
        flash_kernel,
        grid_spec=pltpu.PrefetchScalarGridSpec(
            num_scalar_prefetch=1,
            grid=(seq // BQ,),
            in_specs=[
                pl.BlockSpec((None, BQ, HEAD_DIM), lambda i, e: (0, i, 0)),
                full(1),
                full(2),
            ],
            out_specs=pl.BlockSpec((BQ, HEAD_DIM), lambda i, e: (i, 0)),
        ),
        out_shape=jax.ShapeDtypeStruct((seq, HEAD_DIM), jnp.bfloat16),
    )(ends, qkv, qkv, qkv)


def proj_kernel(mix_ref, att_ref, w_ref, o_ref, acc_ref, mixed_ref):
    i = pl.program_id(0)
    rows = w_ref.shape[0]
    cols = w_ref.shape[1]
    slots = rows // HEAD_DIM

    @pl.when(i == 0)
    def _():
        acc_ref[...] = jnp.zeros_like(acc_ref)

    w = w_ref[...]
    for b in range(PHM_N):
        for s in range(slots):
            part = att_ref[s].astype(jnp.float32) * mix_ref[(i * PHM_N + 0) * PHM_N + b]
            for a in range(1, PHM_N):
                part = part + att_ref[a * slots + s].astype(jnp.float32) * mix_ref[(i * PHM_N + a) * PHM_N + b]
            mixed_ref[:, s * HEAD_DIM:(s + 1) * HEAD_DIM] = part.astype(jnp.bfloat16)
        acc_ref[b] += jnp.dot(mixed_ref[...], w, preferred_element_type=jnp.float32)

    @pl.when(i == PHM_N - 1)
    def _():
        for b in range(PHM_N):
            o_ref[:, b * cols:(b + 1) * cols] = acc_ref[b].astype(o_ref.dtype)


def project(att, mix, w):
    heads, tok, _ = att.shape
    rows = heads * HEAD_DIM // PHM_N
    cols = w.shape[1]
    return pl.pallas_call(
        proj_kernel,
        grid=(PHM_N,),
        in_specs=[
            pl.BlockSpec(memory_space=pltpu.SMEM),
            pl.BlockSpec((heads, tok, HEAD_DIM), lambda i: (0, 0, 0)),
            pl.BlockSpec((rows, cols), lambda i: (i, 0)),
        ],
        out_specs=pl.BlockSpec((tok, PHM_N * cols), lambda i: (0, 0)),
        out_shape=jax.ShapeDtypeStruct((tok, PHM_N * cols), jnp.bfloat16),
        scratch_shapes=[
            pltpu.VMEM((PHM_N, tok, cols), jnp.float32),
            pltpu.VMEM((tok, rows), jnp.bfloat16),
        ],
    )(mix.reshape(-1), att, w)


def body(queries, key_rows, value_rows, doc_blocks, phm_mix, phm_blocks):
    tok_rows = queries.shape[0]
    heads = queries.shape[1] // HEAD_DIM
    factors = lax.all_gather(phm_blocks, "ctx", axis=0, tiled=True)
    stacked = jnp.stack(
        [x.reshape(tok_rows, heads, HEAD_DIM).transpose(1, 0, 2) for x in (queries, key_rows, value_rows)]
    )
    gathered = lax.all_to_all(stacked, "ctx", split_axis=1, concat_axis=1, tiled=True)
    seq_len = heads * tok_rows
    ends = jnp.cumsum(doc_blocks.astype(jnp.int32) * UNIT).astype(jnp.int32)
    attended = attend(gathered.reshape(3, seq_len, HEAD_DIM), ends)
    returned = lax.all_to_all(
        attended.reshape(heads, tok_rows, HEAD_DIM), "ctx", split_axis=0, concat_axis=0, tiled=True
    )
    return project(returned, phm_mix, factors)


def solution(mesh):
    rows = P(("rep", "ctx"), None)
    placed = (rows, rows, rows, P("rep"), P(), P("ctx", None))
    return jax.shard_map(body, mesh=mesh, in_specs=placed, out_specs=rows, check_vma=False)
```

```python
import functools
import math

import jax
import jax.numpy as jnp
from jax import lax
from jax.experimental import pallas as pl
from jax.experimental.pallas import tpu as pltpu
from jax.sharding import PartitionSpec as P

HEAD_DIM = 128
PHM_N = 4
UNIT = 128
BQ = 256
BK = 256


def flash_kernel(ends_ref, q_ref, k_ref, v_ref, o_ref):
    i = pl.program_id(0)
    e0 = ends_ref[0]
    e1 = ends_ref[1]
    scale = 1.0 / math.sqrt(HEAD_DIM)
    per = BK // UNIT

    def doc_start(t):
        return jnp.where(t >= e1, e1, jnp.where(t >= e0, e0, 0))

    q_lo = i * BQ
    q_hi = q_lo + BQ - 1
    j_lo = doc_start(q_lo) // BK
    j_hi = q_hi // BK
    full_lo = (doc_start(q_hi) + BK - 1) // BK
    full_hi = (q_lo + 1) // BK - 1
    mid_lo = jnp.maximum(j_lo, jnp.minimum(full_lo, j_hi + 1))
    mid_hi = jnp.maximum(mid_lo, full_hi + 1)
    q = q_ref[...].reshape(BQ, HEAD_DIM)
    q_pos = q_lo + lax.broadcasted_iota(jnp.int32, (BQ, 1), 0)
    q_start = doc_start(q_pos)

    def step(j, carry, masked):
        m, l, acc = carry
        k = k_ref[pl.ds(j * per, per)].reshape(BK, HEAD_DIM)
        v = v_ref[pl.ds(j * per, per)].reshape(BK, HEAD_DIM)
        s = lax.dot_general(
            q, k, (((1,), (1,)), ((), ())), preferred_element_type=jnp.float32
        ) * scale
        if masked:
            k_pos = j * BK + lax.broadcasted_iota(jnp.int32, (1, BK), 1)
            mask = (k_pos <= q_pos) & (k_pos >= q_start)
            s = jnp.where(mask, s, -1e30)
        m_new = jnp.maximum(m, jnp.max(s, axis=1, keepdims=True))
        p = jnp.exp(s - m_new)
        if masked:
            p = jnp.where(mask, p, 0.0)
        alpha = jnp.exp(m - m_new)
        l = alpha * l + jnp.sum(p, axis=1, keepdims=True)
        acc = alpha * acc + jnp.dot(
            p.astype(jnp.bfloat16), v, preferred_element_type=jnp.float32
        )
        return m_new, l, acc

    carry = (
        jnp.full((BQ, 1), -1e30, jnp.float32),
        jnp.zeros((BQ, 1), jnp.float32),
        jnp.zeros((BQ, HEAD_DIM), jnp.float32),
    )
    edge = functools.partial(step, masked=True)
    inner = functools.partial(step, masked=False)
    carry = lax.fori_loop(j_lo, mid_lo, edge, carry)
    carry = lax.fori_loop(mid_lo, mid_hi, inner, carry)
    m, l, acc = lax.fori_loop(mid_hi, j_hi + 1, edge, carry)
    o_ref[...] = (acc / l).astype(o_ref.dtype)


def attend(qkv, ends):
    blocks = qkv.shape[0]
    seq = blocks * UNIT

    def whole(which):
        return pl.BlockSpec((blocks, None, UNIT, HEAD_DIM), lambda i, e: (0, which, 0, 0))

    return pl.pallas_call(
        flash_kernel,
        grid_spec=pltpu.PrefetchScalarGridSpec(
            num_scalar_prefetch=1,
            grid=(seq // BQ,),
            in_specs=[
                pl.BlockSpec((BQ // UNIT, None, UNIT, HEAD_DIM), lambda i, e: (i, 0, 0, 0)),
                whole(1),
                whole(2),
            ],
            out_specs=pl.BlockSpec((BQ, HEAD_DIM), lambda i, e: (i, 0)),
        ),
        out_shape=jax.ShapeDtypeStruct((seq, HEAD_DIM), jnp.bfloat16),
    )(ends, qkv, qkv, qkv)


def pack_kernel(q_ref, k_ref, v_ref, o_ref):
    for h in range(o_ref.shape[0]):
        for w, x_ref in enumerate((q_ref, k_ref, v_ref)):
            o_ref[h, w] = x_ref[:, h * HEAD_DIM:(h + 1) * HEAD_DIM]


def pack(queries, key_rows, value_rows):
    tok, width = queries.shape
    heads = width // HEAD_DIM
    groups = 4
    per = heads // groups
    spec = pl.BlockSpec((tok, per * HEAD_DIM), lambda g: (0, g))
    return pl.pallas_call(
        pack_kernel,
        grid=(groups,),
        in_specs=[spec, spec, spec],
        out_specs=pl.BlockSpec((per, 3, tok, HEAD_DIM), lambda g: (g, 0, 0, 0)),
        out_shape=jax.ShapeDtypeStruct((heads, 3, tok, HEAD_DIM), queries.dtype),
    )(queries, key_rows, value_rows)


def proj_kernel(mix_ref, att_ref, w_ref, o_ref, acc_ref, mixed_ref):
    i = pl.program_id(0)
    rows = w_ref.shape[0]
    cols = w_ref.shape[1]
    slots = rows // HEAD_DIM

    @pl.when(i == 0)
    def _():
        acc_ref[...] = jnp.zeros_like(acc_ref)

    w = w_ref[...]
    for b in range(PHM_N):
        for s in range(slots):
            part = att_ref[s].astype(jnp.float32) * mix_ref[(i * PHM_N + 0) * PHM_N + b]
            for a in range(1, PHM_N):
                part = part + att_ref[a * slots + s].astype(jnp.float32) * mix_ref[(i * PHM_N + a) * PHM_N + b]
            mixed_ref[:, s * HEAD_DIM:(s + 1) * HEAD_DIM] = part.astype(jnp.bfloat16)
        acc_ref[b] += jnp.dot(mixed_ref[...], w, preferred_element_type=jnp.float32)

    @pl.when(i == PHM_N - 1)
    def _():
        for b in range(PHM_N):
            o_ref[:, b * cols:(b + 1) * cols] = acc_ref[b].astype(o_ref.dtype)


def project(att, mix, w):
    heads, tok, _ = att.shape
    rows = heads * HEAD_DIM // PHM_N
    cols = w.shape[1]
    return pl.pallas_call(
        proj_kernel,
        grid=(PHM_N,),
        in_specs=[
            pl.BlockSpec(memory_space=pltpu.SMEM),
            pl.BlockSpec((heads, tok, HEAD_DIM), lambda i: (0, 0, 0)),
            pl.BlockSpec((rows, cols), lambda i: (i, 0)),
        ],
        out_specs=pl.BlockSpec((tok, PHM_N * cols), lambda i: (0, 0)),
        out_shape=jax.ShapeDtypeStruct((tok, PHM_N * cols), jnp.bfloat16),
        scratch_shapes=[
            pltpu.VMEM((PHM_N, tok, cols), jnp.float32),
            pltpu.VMEM((tok, rows), jnp.bfloat16),
        ],
    )(mix.reshape(-1), att, w)


def body(queries, key_rows, value_rows, doc_blocks, phm_mix, phm_blocks):
    tok_rows = queries.shape[0]
    heads = queries.shape[1] // HEAD_DIM
    factors = lax.all_gather(phm_blocks, "ctx", axis=0, tiled=True)
    stacked = pack(queries, key_rows, value_rows)
    gathered = lax.all_to_all(stacked, "ctx", split_axis=0, concat_axis=0, tiled=True)
    seq_len = heads * tok_rows
    ends = jnp.cumsum(doc_blocks.astype(jnp.int32) * UNIT).astype(jnp.int32)
    attended = attend(gathered, ends)
    returned = lax.all_to_all(
        attended.reshape(heads, tok_rows, HEAD_DIM), "ctx", split_axis=0, concat_axis=0, tiled=True
    )
    return project(returned, phm_mix, factors)


def solution(mesh):
    rows = P(("rep", "ctx"), None)
    placed = (rows, rows, rows, P("rep"), P(), P("ctx", None))
    return jax.shard_map(body, mesh=mesh, in_specs=placed, out_specs=rows, check_vma=False)
```

```python
import functools
import math

import jax
import jax.numpy as jnp
from jax import lax
from jax.experimental import pallas as pl
from jax.experimental.pallas import tpu as pltpu
from jax.sharding import PartitionSpec as P


HEAD_DIM = 128
PHM_N = 4
UNIT = 128
BQ = 256
BK = 256


def flash_kernel(ends_ref, q_ref, k_ref, v_ref, o_ref):
    i = pl.program_id(0)
    e0 = ends_ref[0]
    e1 = ends_ref[1]
    scale = 1.0 / math.sqrt(HEAD_DIM)
    per = BK // UNIT

    def doc_start(t):
        return jnp.where(t >= e1, e1, jnp.where(t >= e0, e0, 0))

    q_lo = i * BQ
    q_hi = q_lo + BQ - 1
    j_lo = doc_start(q_lo) // BK
    j_hi = q_hi // BK
    full_lo = (doc_start(q_hi) + BK - 1) // BK
    full_hi = (q_lo + 1) // BK - 1
    mid_lo = jnp.maximum(j_lo, jnp.minimum(full_lo, j_hi + 1))
    mid_hi = jnp.maximum(mid_lo, full_hi + 1)
    q = q_ref[...].reshape(BQ, HEAD_DIM)
    q_pos = q_lo + lax.broadcasted_iota(jnp.int32, (BQ, 1), 0)
    q_start = doc_start(q_pos)

    def step(j, carry, masked):
        m, l, acc = carry
        k = k_ref[pl.ds(j * per, per)].reshape(BK, HEAD_DIM)
        v = v_ref[pl.ds(j * per, per)].reshape(BK, HEAD_DIM)
        s = lax.dot_general(
            q, k, (((1,), (1,)), ((), ())), preferred_element_type=jnp.float32
        ) * scale
        if masked:
            k_pos = j * BK + lax.broadcasted_iota(jnp.int32, (1, BK), 1)
            mask = (k_pos <= q_pos) & (k_pos >= q_start)
            s = jnp.where(mask, s, -1e30)
        m_new = jnp.maximum(m, jnp.max(s, axis=1, keepdims=True))
        p = jnp.exp(s - m_new)
        if masked:
            p = jnp.where(mask, p, 0.0)
        alpha = jnp.exp(m - m_new)
        l = alpha * l + jnp.sum(p, axis=1, keepdims=True)
        acc = alpha * acc + jnp.dot(
            p.astype(jnp.bfloat16), v, preferred_element_type=jnp.float32
        )
        return m_new, l, acc

    carry = (
        jnp.full((BQ, 1), -1e30, jnp.float32),
        jnp.zeros((BQ, 1), jnp.float32),
        jnp.zeros((BQ, HEAD_DIM), jnp.float32),
    )
    edge = functools.partial(step, masked=True)
    inner = functools.partial(step, masked=False)
    carry = lax.fori_loop(j_lo, mid_lo, edge, carry)
    carry = lax.fori_loop(mid_lo, mid_hi, inner, carry)
    _, l, acc = lax.fori_loop(mid_hi, j_hi + 1, edge, carry)
    o_ref[...] = (acc / l).astype(o_ref.dtype)


def attend(qkv, ends):
    blocks = qkv.shape[0]
    seq = blocks * UNIT

    def whole(which):
        return pl.BlockSpec((blocks, None, UNIT, HEAD_DIM), lambda i, e: (0, which, 0, 0))

    return pl.pallas_call(
        flash_kernel,
        grid_spec=pltpu.PrefetchScalarGridSpec(
            num_scalar_prefetch=1,
            grid=(seq // BQ,),
            in_specs=[
                pl.BlockSpec((BQ // UNIT, None, UNIT, HEAD_DIM), lambda i, e: (i, 0, 0, 0)),
                whole(1),
                whole(2),
            ],
            out_specs=pl.BlockSpec((BQ, HEAD_DIM), lambda i, e: (i, 0)),
        ),
        out_shape=jax.ShapeDtypeStruct((seq, HEAD_DIM), jnp.bfloat16),
    )(ends, qkv, qkv, qkv)


def pack_kernel(q_ref, k_ref, v_ref, o_ref):
    for h in range(o_ref.shape[0]):
        for w, x_ref in enumerate((q_ref, k_ref, v_ref)):
            o_ref[h, w] = x_ref[:, h * HEAD_DIM:(h + 1) * HEAD_DIM]


def pack(queries, key_rows, value_rows):
    tok, width = queries.shape
    heads = width // HEAD_DIM
    groups = 4
    per = heads // groups
    spec = pl.BlockSpec((tok, per * HEAD_DIM), lambda g: (0, g))
    return pl.pallas_call(
        pack_kernel,
        grid=(groups,),
        in_specs=[spec, spec, spec],
        out_specs=pl.BlockSpec((per, 3, tok, HEAD_DIM), lambda g: (g, 0, 0, 0)),
        out_shape=jax.ShapeDtypeStruct((heads, 3, tok, HEAD_DIM), queries.dtype),
    )(queries, key_rows, value_rows)


def proj_kernel(mix_ref, att_ref, w_ref, o_ref, acc_ref, mixed_ref):
    i = pl.program_id(0)
    halves, rows, half_cols = w_ref.shape
    cols = halves * half_cols
    slots = rows // HEAD_DIM

    @pl.when(i == 0)
    def _():
        acc_ref[...] = jnp.zeros_like(acc_ref)

    for b in range(PHM_N):
        for s in range(slots):
            part = att_ref[s].astype(jnp.float32) * mix_ref[(i * PHM_N + 0) * PHM_N + b]
            for a in range(1, PHM_N):
                part = part + att_ref[a * slots + s].astype(jnp.float32) * mix_ref[(i * PHM_N + a) * PHM_N + b]
            mixed_ref[:, s * HEAD_DIM:(s + 1) * HEAD_DIM] = part.astype(jnp.bfloat16)
        mixed = mixed_ref[...]
        for h in range(halves):
            acc_ref[b, :, h * half_cols:(h + 1) * half_cols] += jnp.dot(
                mixed, w_ref[h], preferred_element_type=jnp.float32
            )

    @pl.when(i == PHM_N - 1)
    def _():
        for b in range(PHM_N):
            o_ref[:, b * cols:(b + 1) * cols] = acc_ref[b].astype(o_ref.dtype)


def project(att, mix, w):
    heads, tok, _ = att.shape
    halves, _, half_cols = w.shape
    rows = heads * HEAD_DIM // PHM_N
    cols = halves * half_cols
    return pl.pallas_call(
        proj_kernel,
        grid=(PHM_N,),
        in_specs=[
            pl.BlockSpec(memory_space=pltpu.SMEM),
            pl.BlockSpec((heads, tok, HEAD_DIM), lambda i: (0, 0, 0)),
            pl.BlockSpec((halves, rows, half_cols), lambda i: (0, i, 0)),
        ],
        out_specs=pl.BlockSpec((tok, PHM_N * cols), lambda i: (0, 0)),
        out_shape=jax.ShapeDtypeStruct((tok, PHM_N * cols), jnp.bfloat16),
        scratch_shapes=[
            pltpu.VMEM((PHM_N, tok, cols), jnp.float32),
            pltpu.VMEM((tok, rows), jnp.bfloat16),
        ],
    )(mix.reshape(-1), att, w)


def gather_factors(phm_blocks):
    cols = phm_blocks.shape[1]
    half = cols // lax.axis_size("core")
    mine = lax.dynamic_slice_in_dim(phm_blocks, lax.axis_index("core") * half, half, 1)
    over_ctx = lax.all_gather(mine, "ctx", axis=0, tiled=True)
    return lax.all_gather(over_ctx, "core", axis=0)


def body(queries, key_rows, value_rows, doc_blocks, phm_mix, phm_blocks):
    tok_rows = queries.shape[0]
    heads = queries.shape[1] // HEAD_DIM
    factors = gather_factors(phm_blocks)
    stacked = pack(queries, key_rows, value_rows)
    gathered = lax.all_to_all(stacked, "ctx", split_axis=0, concat_axis=0, tiled=True)
    ends = jnp.cumsum(doc_blocks.astype(jnp.int32) * UNIT).astype(jnp.int32)
    attended = attend(gathered, ends)
    returned = lax.all_to_all(
        attended.reshape(heads, tok_rows, HEAD_DIM), "ctx", split_axis=0, concat_axis=0, tiled=True
    )
    return project(returned, phm_mix, factors)


def solution(mesh):
    rep_at = mesh.axis_names.index("rep")
    shape = list(mesh.devices.shape)
    shape[rep_at:rep_at + 1] = [shape[rep_at] // 2, 2]
    names = list(mesh.axis_names)
    names[rep_at:rep_at + 1] = ["x", "core"]
    split = jax.sharding.Mesh(mesh.devices.reshape(shape), tuple(names))
    rows = P(("x", "core", "ctx"), None)
    placed = (rows, rows, rows, P(("x", "core")), P(), P("ctx", None))
    return jax.shard_map(body, mesh=split, in_specs=placed, out_specs=rows, check_vma=False)
```

```python
import functools
import math

import jax
import jax.numpy as jnp
from jax import lax
from jax.experimental import pallas as pl
from jax.experimental.pallas import tpu as pltpu
from jax.sharding import PartitionSpec as P


HEAD_DIM = 128
PHM_N = 4
UNIT = 128
BQ = 512
BK = 256


def flash_kernel(ends_ref, q_ref, k_ref, v_ref, o_ref):
    i = pl.program_id(0)
    e0 = ends_ref[0]
    e1 = ends_ref[1]
    scale = 1.0 / math.sqrt(HEAD_DIM)
    per = BK // UNIT

    def doc_start(t):
        return jnp.where(t >= e1, e1, jnp.where(t >= e0, e0, 0))

    q_lo = i * BQ
    q_hi = q_lo + BQ - 1
    j_lo = doc_start(q_lo) // BK
    j_hi = q_hi // BK
    full_lo = (doc_start(q_hi) + BK - 1) // BK
    full_hi = (q_lo + 1) // BK - 1
    mid_lo = jnp.maximum(j_lo, jnp.minimum(full_lo, j_hi + 1))
    mid_hi = jnp.maximum(mid_lo, full_hi + 1)
    q = q_ref[...].reshape(BQ, HEAD_DIM)
    q_pos = q_lo + lax.broadcasted_iota(jnp.int32, (BQ, 1), 0)
    q_start = doc_start(q_pos)

    def step(j, carry, masked):
        m, l, acc = carry
        k = k_ref[pl.ds(j * per, per)].reshape(BK, HEAD_DIM)
        v = v_ref[pl.ds(j * per, per)].reshape(BK, HEAD_DIM)
        s = lax.dot_general(
            q, k, (((1,), (1,)), ((), ())), preferred_element_type=jnp.float32
        ) * scale
        if masked:
            k_pos = j * BK + lax.broadcasted_iota(jnp.int32, (1, BK), 1)
            mask = (k_pos <= q_pos) & (k_pos >= q_start)
            s = jnp.where(mask, s, -1e30)
        m_new = jnp.maximum(m, jnp.max(s, axis=1, keepdims=True))
        p = jnp.exp(s - m_new)
        if masked:
            p = jnp.where(mask, p, 0.0)
        alpha = jnp.exp(m - m_new)
        l = alpha * l + jnp.sum(p, axis=1, keepdims=True)
        acc = alpha * acc + jnp.dot(
            p.astype(jnp.bfloat16), v, preferred_element_type=jnp.float32
        )
        return m_new, l, acc

    carry = (
        jnp.full((BQ, 1), -1e30, jnp.float32),
        jnp.zeros((BQ, 1), jnp.float32),
        jnp.zeros((BQ, HEAD_DIM), jnp.float32),
    )
    edge = functools.partial(step, masked=True)
    inner = functools.partial(step, masked=False)
    carry = lax.fori_loop(j_lo, mid_lo, edge, carry)
    carry = lax.fori_loop(mid_lo, mid_hi, inner, carry)
    _, l, acc = lax.fori_loop(mid_hi, j_hi + 1, edge, carry)
    o_ref[...] = (acc / l).astype(o_ref.dtype)


def attend(qkv, ends):
    blocks = qkv.shape[0]
    seq = blocks * UNIT

    def whole(which):
        return pl.BlockSpec((blocks, None, UNIT, HEAD_DIM), lambda i, e: (0, which, 0, 0))

    return pl.pallas_call(
        flash_kernel,
        grid_spec=pltpu.PrefetchScalarGridSpec(
            num_scalar_prefetch=1,
            grid=(seq // BQ,),
            in_specs=[
                pl.BlockSpec((BQ // UNIT, None, UNIT, HEAD_DIM), lambda i, e: (i, 0, 0, 0)),
                whole(1),
                whole(2),
            ],
            out_specs=pl.BlockSpec((BQ, HEAD_DIM), lambda i, e: (i, 0)),
        ),
        out_shape=jax.ShapeDtypeStruct((seq, HEAD_DIM), jnp.bfloat16),
    )(ends, qkv, qkv, qkv)


def pack_kernel(q_ref, k_ref, v_ref, o_ref):
    for h in range(o_ref.shape[0]):
        for w, x_ref in enumerate((q_ref, k_ref, v_ref)):
            o_ref[h, w] = x_ref[:, h * HEAD_DIM:(h + 1) * HEAD_DIM]


def pack(queries, key_rows, value_rows):
    tok, width = queries.shape
    heads = width // HEAD_DIM
    groups = 4
    per = heads // groups
    spec = pl.BlockSpec((tok, per * HEAD_DIM), lambda g: (0, g))
    return pl.pallas_call(
        pack_kernel,
        grid=(groups,),
        in_specs=[spec, spec, spec],
        out_specs=pl.BlockSpec((per, 3, tok, HEAD_DIM), lambda g: (g, 0, 0, 0)),
        out_shape=jax.ShapeDtypeStruct((heads, 3, tok, HEAD_DIM), queries.dtype),
    )(queries, key_rows, value_rows)


def proj_kernel(mix_ref, att_ref, w_ref, o_ref, acc_ref, mixed_ref, wide_ref):
    i = pl.program_id(0)
    halves, rows, half_cols = w_ref.shape
    cols = halves * half_cols
    slots = rows // HEAD_DIM

    @pl.when(i == 0)
    def _():
        acc_ref[...] = jnp.zeros_like(acc_ref)
        for h in range(att_ref.shape[0]):
            wide_ref[h] = att_ref[h].astype(jnp.float32)

    for b in range(PHM_N):
        for s in range(slots):
            part = wide_ref[s] * mix_ref[(i * PHM_N + 0) * PHM_N + b]
            for a in range(1, PHM_N):
                part = part + wide_ref[a * slots + s] * mix_ref[(i * PHM_N + a) * PHM_N + b]
            mixed_ref[:, s * HEAD_DIM:(s + 1) * HEAD_DIM] = part.astype(jnp.bfloat16)
        mixed = mixed_ref[...]
        for h in range(halves):
            acc_ref[b, :, h * half_cols:(h + 1) * half_cols] += jnp.dot(
                mixed, w_ref[h], preferred_element_type=jnp.float32
            )

    @pl.when(i == PHM_N - 1)
    def _():
        for b in range(PHM_N):
            o_ref[:, b * cols:(b + 1) * cols] = acc_ref[b].astype(o_ref.dtype)


def project(att, mix, w):
    heads, tok, _ = att.shape
    halves, _, half_cols = w.shape
    rows = heads * HEAD_DIM // PHM_N
    cols = halves * half_cols
    return pl.pallas_call(
        proj_kernel,
        grid=(PHM_N,),
        in_specs=[
            pl.BlockSpec(memory_space=pltpu.SMEM),
            pl.BlockSpec((heads, tok, HEAD_DIM), lambda i: (0, 0, 0)),
            pl.BlockSpec((halves, rows, half_cols), lambda i: (0, i, 0)),
        ],
        out_specs=pl.BlockSpec((tok, PHM_N * cols), lambda i: (0, 0)),
        out_shape=jax.ShapeDtypeStruct((tok, PHM_N * cols), jnp.bfloat16),
        scratch_shapes=[
            pltpu.VMEM((PHM_N, tok, cols), jnp.float32),
            pltpu.VMEM((tok, rows), jnp.bfloat16),
            pltpu.VMEM((heads, tok, HEAD_DIM), jnp.float32),
        ],
    )(mix.reshape(-1), att, w)


def gather_factors(phm_blocks):
    cols = phm_blocks.shape[1]
    half = cols // lax.axis_size("core")
    mine = lax.dynamic_slice_in_dim(phm_blocks, lax.axis_index("core") * half, half, 1)
    over_ctx = lax.all_gather(mine, "ctx", axis=0, tiled=True)
    return lax.all_gather(over_ctx, "core", axis=0)


def body(queries, key_rows, value_rows, doc_blocks, phm_mix, phm_blocks):
    tok_rows = queries.shape[0]
    heads = queries.shape[1] // HEAD_DIM
    factors = gather_factors(phm_blocks)
    stacked = pack(queries, key_rows, value_rows)
    gathered = lax.all_to_all(stacked, "ctx", split_axis=0, concat_axis=0, tiled=True)
    ends = jnp.cumsum(doc_blocks.astype(jnp.int32) * UNIT).astype(jnp.int32)
    attended = attend(gathered, ends)
    returned = lax.all_to_all(
        attended.reshape(heads, tok_rows, HEAD_DIM), "ctx", split_axis=0, concat_axis=0, tiled=True
    )
    return project(returned, phm_mix, factors)


def solution(mesh):
    rep_at = mesh.axis_names.index("rep")
    shape = list(mesh.devices.shape)
    shape[rep_at:rep_at + 1] = [shape[rep_at] // 2, 2]
    names = list(mesh.axis_names)
    names[rep_at:rep_at + 1] = ["x", "core"]
    split = jax.sharding.Mesh(mesh.devices.reshape(shape), tuple(names))
    rows = P(("x", "core", "ctx"), None)
    placed = (rows, rows, rows, P(("x", "core")), P(), P("ctx", None))
    return jax.shard_map(body, mesh=split, in_specs=placed, out_specs=rows, check_vma=False)
```

```python
import functools
import math

import jax
import jax.numpy as jnp
from jax import lax
from jax.experimental import pallas as pl
from jax.experimental.pallas import tpu as pltpu
from jax.sharding import PartitionSpec as P


HEAD_DIM = 128
PHM_N = 4
UNIT = 128
BQ = 1024
PHASES = 2
BK = 256


def flash_kernel(ends_ref, q_ref, k_ref, v_ref, o_ref, *, phase):
    g = pl.program_id(0)
    e0 = ends_ref[0]
    e1 = ends_ref[1]
    scale = 1.0 / math.sqrt(HEAD_DIM)
    per = BK // UNIT
    dests, half, _ = q_ref.shape
    rows = dests * half

    def doc_start(t):
        return jnp.where(t >= e1, e1, jnp.where(t >= e0, e0, 0))

    q_lo = g * dests * UNIT + phase * half
    q_hi = q_lo + (dests - 1) * UNIT + half - 1
    j_lo = doc_start(q_lo) // BK
    j_hi = q_hi // BK
    full_lo = (doc_start(q_hi) + BK - 1) // BK
    full_hi = (q_lo + 1) // BK - 1
    mid_lo = jnp.maximum(j_lo, jnp.minimum(full_lo, j_hi + 1))
    mid_hi = jnp.maximum(mid_lo, full_hi + 1)
    q = q_ref[...].reshape(rows, HEAD_DIM)
    r = lax.broadcasted_iota(jnp.int32, (rows, 1), 0)
    q_pos = q_lo + (r // half) * UNIT + r % half
    q_start = doc_start(q_pos)

    def step(j, carry, masked):
        m, l, acc = carry
        k = k_ref[pl.ds(j * per, per)].reshape(BK, HEAD_DIM)
        v = v_ref[pl.ds(j * per, per)].reshape(BK, HEAD_DIM)
        s = lax.dot_general(
            q, k, (((1,), (1,)), ((), ())), preferred_element_type=jnp.float32
        ) * scale
        if masked:
            k_pos = j * BK + lax.broadcasted_iota(jnp.int32, (1, BK), 1)
            mask = (k_pos <= q_pos) & (k_pos >= q_start)
            s = jnp.where(mask, s, -1e30)
        m_new = jnp.maximum(m, jnp.max(s, axis=1, keepdims=True))
        p = jnp.exp(s - m_new)
        if masked:
            p = jnp.where(mask, p, 0.0)
        alpha = jnp.exp(m - m_new)
        l = alpha * l + jnp.sum(p, axis=1, keepdims=True)
        acc = alpha * acc + jnp.dot(
            p.astype(jnp.bfloat16), v, preferred_element_type=jnp.float32
        )
        return m_new, l, acc

    carry = (
        jnp.full((rows, 1), -1e30, jnp.float32),
        jnp.zeros((rows, 1), jnp.float32),
        jnp.zeros((rows, HEAD_DIM), jnp.float32),
    )
    edge = functools.partial(step, masked=True)
    inner = functools.partial(step, masked=False)
    carry = lax.fori_loop(j_lo, mid_lo, edge, carry)
    carry = lax.fori_loop(mid_lo, mid_hi, inner, carry)
    _, l, acc = lax.fori_loop(mid_hi, j_hi + 1, edge, carry)
    o_ref[...] = (acc / l).astype(o_ref.dtype).reshape(dests, half, HEAD_DIM)


def attend(qkv, ends, phase):
    blocks = qkv.shape[0]
    half = UNIT // PHASES
    dests = BQ // UNIT
    split = qkv.reshape(blocks, 3, PHASES, half, HEAD_DIM)

    def whole(which):
        return pl.BlockSpec(
            (blocks, None, PHASES, half, HEAD_DIM), lambda g, e: (0, which, 0, 0, 0)
        )

    return pl.pallas_call(
        functools.partial(flash_kernel, phase=phase),
        grid_spec=pltpu.PrefetchScalarGridSpec(
            num_scalar_prefetch=1,
            grid=(blocks // dests,),
            in_specs=[
                pl.BlockSpec(
                    (dests, None, None, half, HEAD_DIM), lambda g, e: (g, 0, phase, 0, 0)
                ),
                whole(1),
                whole(2),
            ],
            out_specs=pl.BlockSpec((dests, half, HEAD_DIM), lambda g, e: (g, 0, 0)),
        ),
        out_shape=jax.ShapeDtypeStruct((blocks, half, HEAD_DIM), jnp.bfloat16),
    )(ends, split, split, split)


def pack_kernel(q_ref, k_ref, v_ref, o_ref):
    for h in range(o_ref.shape[0]):
        for w, x_ref in enumerate((q_ref, k_ref, v_ref)):
            o_ref[h, w] = x_ref[:, h * HEAD_DIM:(h + 1) * HEAD_DIM]


def pack(queries, key_rows, value_rows):
    tok, width = queries.shape
    heads = width // HEAD_DIM
    groups = 4
    per = heads // groups
    spec = pl.BlockSpec((tok, per * HEAD_DIM), lambda g: (0, g))
    return pl.pallas_call(
        pack_kernel,
        grid=(groups,),
        in_specs=[spec, spec, spec],
        out_specs=pl.BlockSpec((per, 3, tok, HEAD_DIM), lambda g: (g, 0, 0, 0)),
        out_shape=jax.ShapeDtypeStruct((heads, 3, tok, HEAD_DIM), queries.dtype),
    )(queries, key_rows, value_rows)


def proj_kernel(mix_ref, att_ref, w_ref, o_ref, acc_ref, mixed_ref, wide_ref):
    i = pl.program_id(0)
    halves, rows, half_cols = w_ref.shape
    cols = halves * half_cols
    slots = rows // HEAD_DIM

    @pl.when(i == 0)
    def _():
        acc_ref[...] = jnp.zeros_like(acc_ref)
        for h in range(att_ref.shape[0]):
            wide_ref[h] = att_ref[h].astype(jnp.float32)

    for b in range(PHM_N):
        for s in range(slots):
            part = wide_ref[s] * mix_ref[(i * PHM_N + 0) * PHM_N + b]
            for a in range(1, PHM_N):
                part = part + wide_ref[a * slots + s] * mix_ref[(i * PHM_N + a) * PHM_N + b]
            mixed_ref[:, s * HEAD_DIM:(s + 1) * HEAD_DIM] = part.astype(jnp.bfloat16)
        mixed = mixed_ref[...]
        for h in range(halves):
            acc_ref[b, :, h * half_cols:(h + 1) * half_cols] += jnp.dot(
                mixed, w_ref[h], preferred_element_type=jnp.float32
            )

    @pl.when(i == PHM_N - 1)
    def _():
        for b in range(PHM_N):
            o_ref[:, b * cols:(b + 1) * cols] = acc_ref[b].astype(o_ref.dtype)


def project(att, mix, w):
    heads, tok, _ = att.shape
    halves, _, half_cols = w.shape
    rows = heads * HEAD_DIM // PHM_N
    cols = halves * half_cols
    return pl.pallas_call(
        proj_kernel,
        grid=(PHM_N,),
        in_specs=[
            pl.BlockSpec(memory_space=pltpu.SMEM),
            pl.BlockSpec((heads, tok, HEAD_DIM), lambda i: (0, 0, 0)),
            pl.BlockSpec((halves, rows, half_cols), lambda i: (0, i, 0)),
        ],
        out_specs=pl.BlockSpec((tok, PHM_N * cols), lambda i: (0, 0)),
        out_shape=jax.ShapeDtypeStruct((tok, PHM_N * cols), jnp.bfloat16),
        scratch_shapes=[
            pltpu.VMEM((PHM_N, tok, cols), jnp.float32),
            pltpu.VMEM((tok, rows), jnp.bfloat16),
            pltpu.VMEM((heads, tok, HEAD_DIM), jnp.float32),
        ],
    )(mix.reshape(-1), att, w)


def gather_factors(phm_blocks):
    cols = phm_blocks.shape[1]
    half = cols // lax.axis_size("core")
    mine = lax.dynamic_slice_in_dim(phm_blocks, lax.axis_index("core") * half, half, 1)
    over_ctx = lax.all_gather(mine, "ctx", axis=0, tiled=True)
    return lax.all_gather(over_ctx, "core", axis=0)


def body(queries, key_rows, value_rows, doc_blocks, phm_mix, phm_blocks):
    factors = gather_factors(phm_blocks)
    stacked = pack(queries, key_rows, value_rows)
    gathered = lax.all_to_all(stacked, "ctx", split_axis=0, concat_axis=0, tiled=True)
    ends = jnp.cumsum(doc_blocks.astype(jnp.int32) * UNIT).astype(jnp.int32)
    returned = []
    for phase in range(PHASES):
        attended = attend(gathered, ends, phase)
        returned.append(lax.all_to_all(attended, "ctx", split_axis=0, concat_axis=0, tiled=True))
    returned = jnp.concatenate(returned, axis=1)
    return project(returned, phm_mix, factors)


def solution(mesh):
    rep_at = mesh.axis_names.index("rep")
    shape = list(mesh.devices.shape)
    shape[rep_at:rep_at + 1] = [shape[rep_at] // 2, 2]
    names = list(mesh.axis_names)
    names[rep_at:rep_at + 1] = ["x", "core"]
    split = jax.sharding.Mesh(mesh.devices.reshape(shape), tuple(names))
    rows = P(("x", "core", "ctx"), None)
    placed = (rows, rows, rows, P(("x", "core")), P(), P("ctx", None))
    return jax.shard_map(body, mesh=split, in_specs=placed, out_specs=rows, check_vma=False)
```

```python
import functools
import math

import jax
import jax.numpy as jnp
from jax import lax
from jax.experimental import pallas as pl
from jax.experimental.pallas import tpu as pltpu
from jax.sharding import PartitionSpec as P


HEAD_DIM = 128
PHM_N = 4
UNIT = 128
BQ = 512
BK = 256


def flash_kernel(ends_ref, q_ref, k_ref, v_ref, o_ref):
    i = pl.program_id(0)
    e0 = ends_ref[0]
    e1 = ends_ref[1]
    scale = 1.0 / math.sqrt(HEAD_DIM)
    per = BK // UNIT

    def doc_start(t):
        return jnp.where(t >= e1, e1, jnp.where(t >= e0, e0, 0))

    q_lo = i * BQ
    q_hi = q_lo + BQ - 1
    j_lo = doc_start(q_lo) // BK
    j_hi = q_hi // BK
    full_lo = (doc_start(q_hi) + BK - 1) // BK
    full_hi = (q_lo + 1) // BK - 1
    mid_lo = jnp.maximum(j_lo, jnp.minimum(full_lo, j_hi + 1))
    mid_hi = jnp.maximum(mid_lo, full_hi + 1)
    q = q_ref[...].reshape(BQ, HEAD_DIM)
    q_pos = q_lo + lax.broadcasted_iota(jnp.int32, (BQ, 1), 0)
    q_start = doc_start(q_pos)

    def step(j, carry, masked):
        m, l, acc = carry
        k = k_ref[pl.ds(j * per, per)].reshape(BK, HEAD_DIM)
        v = v_ref[pl.ds(j * per, per)].reshape(BK, HEAD_DIM)
        s = lax.dot_general(
            q, k, (((1,), (1,)), ((), ())), preferred_element_type=jnp.float32
        ) * scale
        if masked:
            k_pos = j * BK + lax.broadcasted_iota(jnp.int32, (1, BK), 1)
            mask = k_pos <= q_pos
            if masked == "both":
                mask = mask & (k_pos >= q_start)
            s = jnp.where(mask, s, -jnp.inf)
        m_new = jnp.maximum(m, jnp.max(s, axis=1, keepdims=True))
        p = jnp.exp(s - m_new)
        alpha = jnp.exp(m - m_new)
        l = alpha * l + jnp.sum(p, axis=1, keepdims=True)
        acc = alpha * acc + jnp.dot(
            p.astype(jnp.bfloat16), v, preferred_element_type=jnp.float32
        )
        return m_new, l, acc

    carry = (
        jnp.full((BQ, 1), -1e30, jnp.float32),
        jnp.zeros((BQ, 1), jnp.float32),
        jnp.zeros((BQ, HEAD_DIM), jnp.float32),
    )
    edge = functools.partial(step, masked="both")
    inner = functools.partial(step, masked=None)
    diagonal = functools.partial(step, masked="causal")
    carry = lax.fori_loop(j_lo, mid_lo, edge, carry)
    carry = lax.fori_loop(mid_lo, mid_hi, inner, carry)
    _, l, acc = lax.fori_loop(mid_hi, j_hi + 1, diagonal, carry)
    o_ref[...] = (acc / l).astype(o_ref.dtype)


def attend(qkv, ends):
    blocks = qkv.shape[0]
    seq = blocks * UNIT

    def whole(which):
        return pl.BlockSpec((blocks, None, UNIT, HEAD_DIM), lambda i, e: (0, which, 0, 0))

    return pl.pallas_call(
        flash_kernel,
        grid_spec=pltpu.PrefetchScalarGridSpec(
            num_scalar_prefetch=1,
            grid=(seq // BQ,),
            in_specs=[
                pl.BlockSpec((BQ // UNIT, None, UNIT, HEAD_DIM), lambda i, e: (i, 0, 0, 0)),
                whole(1),
                whole(2),
            ],
            out_specs=pl.BlockSpec((BQ, HEAD_DIM), lambda i, e: (i, 0)),
        ),
        out_shape=jax.ShapeDtypeStruct((seq, HEAD_DIM), jnp.bfloat16),
    )(ends, qkv, qkv, qkv)


def pack_kernel(q_ref, k_ref, v_ref, o_ref):
    for h in range(o_ref.shape[0]):
        for w, x_ref in enumerate((q_ref, k_ref, v_ref)):
            o_ref[h, w] = x_ref[:, h * HEAD_DIM:(h + 1) * HEAD_DIM]


def pack(queries, key_rows, value_rows):
    tok, width = queries.shape
    heads = width // HEAD_DIM
    groups = 2
    per = heads // groups
    spec = pl.BlockSpec((tok, per * HEAD_DIM), lambda g: (0, g))
    return pl.pallas_call(
        pack_kernel,
        grid=(groups,),
        in_specs=[spec, spec, spec],
        out_specs=pl.BlockSpec((per, 3, tok, HEAD_DIM), lambda g: (g, 0, 0, 0)),
        out_shape=jax.ShapeDtypeStruct((heads, 3, tok, HEAD_DIM), queries.dtype),
    )(queries, key_rows, value_rows)


def proj_kernel(mix_ref, att_ref, w_ref, o_ref, acc_ref, mixed_ref, wide_ref):
    i = pl.program_id(0)
    halves, rows, half_cols = w_ref.shape
    cols = halves * half_cols
    slots = rows // HEAD_DIM

    @pl.when(i == 0)
    def _():
        acc_ref[...] = jnp.zeros_like(acc_ref)
        for h in range(att_ref.shape[0]):
            wide_ref[h] = att_ref[h].astype(jnp.float32)

    for b in range(PHM_N):
        for s in range(slots):
            part = wide_ref[s] * mix_ref[(i * PHM_N + 0) * PHM_N + b]
            for a in range(1, PHM_N):
                part = part + wide_ref[a * slots + s] * mix_ref[(i * PHM_N + a) * PHM_N + b]
            mixed_ref[:, s * HEAD_DIM:(s + 1) * HEAD_DIM] = part.astype(jnp.bfloat16)
        mixed = mixed_ref[...]
        for h in range(halves):
            acc_ref[b, :, h * half_cols:(h + 1) * half_cols] += jnp.dot(
                mixed, w_ref[h], preferred_element_type=jnp.float32
            )

    @pl.when(i == PHM_N - 1)
    def _():
        for b in range(PHM_N):
            o_ref[:, b * cols:(b + 1) * cols] = acc_ref[b].astype(o_ref.dtype)


def project(att, mix, w):
    heads, tok, _ = att.shape
    halves, _, half_cols = w.shape
    rows = heads * HEAD_DIM // PHM_N
    cols = halves * half_cols
    return pl.pallas_call(
        proj_kernel,
        grid=(PHM_N,),
        in_specs=[
            pl.BlockSpec(memory_space=pltpu.SMEM),
            pl.BlockSpec((heads, tok, HEAD_DIM), lambda i: (0, 0, 0)),
            pl.BlockSpec((halves, rows, half_cols), lambda i: (0, i, 0)),
        ],
        out_specs=pl.BlockSpec((tok, PHM_N * cols), lambda i: (0, 0)),
        out_shape=jax.ShapeDtypeStruct((tok, PHM_N * cols), jnp.bfloat16),
        scratch_shapes=[
            pltpu.VMEM((PHM_N, tok, cols), jnp.float32),
            pltpu.VMEM((tok, rows), jnp.bfloat16),
            pltpu.VMEM((heads, tok, HEAD_DIM), jnp.float32),
        ],
    )(mix.reshape(-1), att, w)


def gather_factors(phm_blocks):
    cols = phm_blocks.shape[1]
    half = cols // lax.axis_size("core")
    mine = lax.dynamic_slice_in_dim(phm_blocks, lax.axis_index("core") * half, half, 1)
    over_ctx = lax.all_gather(mine, "ctx", axis=0, tiled=True)
    return lax.all_gather(over_ctx, "core", axis=0)


def body(queries, key_rows, value_rows, doc_blocks, phm_mix, phm_blocks):
    tok_rows = queries.shape[0]
    heads = queries.shape[1] // HEAD_DIM
    factors = gather_factors(phm_blocks)
    stacked = pack(queries, key_rows, value_rows)
    gathered = lax.all_to_all(stacked, "ctx", split_axis=0, concat_axis=0, tiled=True)
    ends = jnp.cumsum(doc_blocks.astype(jnp.int32) * UNIT).astype(jnp.int32)
    attended = attend(gathered, ends)
    returned = lax.all_to_all(
        attended.reshape(heads, tok_rows, HEAD_DIM), "ctx", split_axis=0, concat_axis=0, tiled=True
    )
    return project(returned, phm_mix, factors)


def solution(mesh):
    rep_at = mesh.axis_names.index("rep")
    shape = list(mesh.devices.shape)
    shape[rep_at:rep_at + 1] = [shape[rep_at] // 2, 2]
    names = list(mesh.axis_names)
    names[rep_at:rep_at + 1] = ["x", "core"]
    split = jax.sharding.Mesh(mesh.devices.reshape(shape), tuple(names))
    rows = P(("x", "core", "ctx"), None)
    placed = (rows, rows, rows, P(("x", "core")), P(), P("ctx", None))
    return jax.shard_map(body, mesh=split, in_specs=placed, out_specs=rows, check_vma=False)
```

```python
import functools
import math

import jax
import jax.numpy as jnp
from jax import lax
from jax.experimental import pallas as pl
from jax.experimental.pallas import tpu as pltpu
from jax.sharding import PartitionSpec as P


HEAD_DIM = 128
PHM_N = 4
UNIT = 128
BQ = 512
BK = 256


def flash_kernel(ends_ref, q_ref, k_ref, v_ref, o_ref):
    i = pl.program_id(0)
    e0 = ends_ref[0]
    e1 = ends_ref[1]
    scale = 1.0 / math.sqrt(HEAD_DIM)
    per = BK // UNIT

    def doc_start(t):
        return jnp.where(t >= e1, e1, jnp.where(t >= e0, e0, 0))

    q_lo = i * BQ
    q_hi = q_lo + BQ - 1
    j_lo = doc_start(q_lo) // BK
    j_hi = q_hi // BK
    full_lo = (doc_start(q_hi) + BK - 1) // BK
    full_hi = (q_lo + 1) // BK - 1
    mid_lo = jnp.maximum(j_lo, jnp.minimum(full_lo, j_hi + 1))
    mid_hi = jnp.maximum(mid_lo, full_hi + 1)
    q = q_ref[...].reshape(BQ, HEAD_DIM)
    q_pos = q_lo + lax.broadcasted_iota(jnp.int32, (BQ, 1), 0)
    q_start = doc_start(q_pos)

    def step(j, carry, masked):
        m, l, acc = carry
        k = k_ref[pl.ds(j * per, per)].reshape(BK, HEAD_DIM)
        v = v_ref[pl.ds(j * per, per)].reshape(BK, HEAD_DIM)
        s = lax.dot_general(
            q, k, (((1,), (1,)), ((), ())), preferred_element_type=jnp.float32
        ) * scale
        if masked:
            k_pos = j * BK + lax.broadcasted_iota(jnp.int32, (1, BK), 1)
            mask = k_pos <= q_pos
            if masked == "both":
                mask = mask & (k_pos >= q_start)
            s = jnp.where(mask, s, -jnp.inf)
        m_new = jnp.maximum(m, jnp.max(s, axis=1, keepdims=True))
        p = jnp.exp(s - m_new)
        alpha = jnp.exp(m - m_new)
        l = alpha * l + jnp.sum(p, axis=1, keepdims=True)
        acc = alpha * acc + jnp.dot(
            p.astype(jnp.bfloat16), v, preferred_element_type=jnp.float32
        )
        return m_new, l, acc

    carry = (
        jnp.full((BQ, 1), -1e30, jnp.float32),
        jnp.zeros((BQ, 1), jnp.float32),
        jnp.zeros((BQ, HEAD_DIM), jnp.float32),
    )
    edge = functools.partial(step, masked="both")
    inner = functools.partial(step, masked=None)
    diagonal = functools.partial(step, masked="causal")
    carry = lax.fori_loop(j_lo, mid_lo, edge, carry)
    carry = lax.fori_loop(mid_lo, mid_hi, inner, carry)
    _, l, acc = lax.fori_loop(mid_hi, j_hi + 1, diagonal, carry)
    o_ref[...] = (acc / l).astype(o_ref.dtype)


def attend(qkv, ends):
    blocks = qkv.shape[0]
    seq = blocks * UNIT

    def whole(which):
        return pl.BlockSpec((blocks, None, UNIT, HEAD_DIM), lambda i, e: (0, which, 0, 0))

    return pl.pallas_call(
        flash_kernel,
        grid_spec=pltpu.PrefetchScalarGridSpec(
            num_scalar_prefetch=1,
            grid=(seq // BQ,),
            in_specs=[
                pl.BlockSpec((BQ // UNIT, None, UNIT, HEAD_DIM), lambda i, e: (i, 0, 0, 0)),
                whole(1),
                whole(2),
            ],
            out_specs=pl.BlockSpec((BQ, HEAD_DIM), lambda i, e: (i, 0)),
        ),
        out_shape=jax.ShapeDtypeStruct((seq, HEAD_DIM), jnp.bfloat16),
    )(ends, qkv, qkv, qkv)


def pack_kernel(q_ref, k_ref, v_ref, o_ref):
    for h in range(o_ref.shape[0]):
        for w, x_ref in enumerate((q_ref, k_ref, v_ref)):
            o_ref[h, w] = x_ref[:, h * HEAD_DIM:(h + 1) * HEAD_DIM]


def pack(queries, key_rows, value_rows):
    tok, width = queries.shape
    heads = width // HEAD_DIM
    groups = 2
    per = heads // groups
    spec = pl.BlockSpec((tok, per * HEAD_DIM), lambda g: (0, g))
    return pl.pallas_call(
        pack_kernel,
        grid=(groups,),
        in_specs=[spec, spec, spec],
        out_specs=pl.BlockSpec((per, 3, tok, HEAD_DIM), lambda g: (g, 0, 0, 0)),
        out_shape=jax.ShapeDtypeStruct((heads, 3, tok, HEAD_DIM), queries.dtype),
    )(queries, key_rows, value_rows)


def proj_kernel(mix_ref, att_ref, w_ref, o_ref, acc_ref, mixed_ref, wide_ref):
    i = pl.program_id(0)
    halves, rows, half_cols = w_ref.shape
    cols = halves * half_cols
    slots = rows // HEAD_DIM

    @pl.when(i == 0)
    def _():
        acc_ref[...] = jnp.zeros_like(acc_ref)
        for h in range(att_ref.shape[0]):
            wide_ref[h] = att_ref[h].astype(jnp.float32)

    for b in range(PHM_N):
        for s in range(slots):
            part = wide_ref[s] * mix_ref[(i * PHM_N + 0) * PHM_N + b]
            for a in range(1, PHM_N):
                part = part + wide_ref[a * slots + s] * mix_ref[(i * PHM_N + a) * PHM_N + b]
            mixed_ref[:, s * HEAD_DIM:(s + 1) * HEAD_DIM] = part.astype(jnp.bfloat16)
        mixed = mixed_ref[...]
        for h in range(halves):
            acc_ref[b, :, h * half_cols:(h + 1) * half_cols] += jnp.dot(
                mixed, w_ref[h], preferred_element_type=jnp.float32
            )

    @pl.when(i == PHM_N - 1)
    def _():
        for b in range(PHM_N):
            o_ref[:, b * cols:(b + 1) * cols] = acc_ref[b].astype(o_ref.dtype)


def project(att, mix, w):
    heads, tok, _ = att.shape
    halves, _, half_cols = w.shape
    rows = heads * HEAD_DIM // PHM_N
    cols = halves * half_cols
    return pl.pallas_call(
        proj_kernel,
        grid=(PHM_N,),
        in_specs=[
            pl.BlockSpec(memory_space=pltpu.SMEM),
            pl.BlockSpec((heads, tok, HEAD_DIM), lambda i: (0, 0, 0)),
            pl.BlockSpec((halves, rows, half_cols), lambda i: (0, i, 0)),
        ],
        out_specs=pl.BlockSpec((tok, PHM_N * cols), lambda i: (0, 0)),
        out_shape=jax.ShapeDtypeStruct((tok, PHM_N * cols), jnp.bfloat16),
        scratch_shapes=[
            pltpu.VMEM((PHM_N, tok, cols), jnp.float32),
            pltpu.VMEM((tok, rows), jnp.bfloat16),
            pltpu.VMEM((heads, tok, HEAD_DIM), jnp.float32),
        ],
    )(mix.reshape(-1), att, w)


def gather_factors(phm_blocks):
    over_ctx = lax.all_gather(phm_blocks, "ctx", axis=0, tiled=True)
    return over_ctx[None]


def body(queries, key_rows, value_rows, doc_blocks, phm_mix, phm_blocks):
    tok_rows = queries.shape[0]
    heads = queries.shape[1] // HEAD_DIM
    factors = gather_factors(phm_blocks)
    stacked = pack(queries, key_rows, value_rows)
    gathered = lax.all_to_all(stacked, "ctx", split_axis=0, concat_axis=0, tiled=True)
    ends = jnp.cumsum(doc_blocks.astype(jnp.int32) * UNIT).astype(jnp.int32)
    attended = attend(gathered, ends)
    returned = lax.all_to_all(
        attended.reshape(heads, tok_rows, HEAD_DIM), "ctx", split_axis=0, concat_axis=0, tiled=True
    )
    return project(returned, phm_mix, factors)


def solution(mesh):
    rep_at = mesh.axis_names.index("rep")
    shape = list(mesh.devices.shape)
    shape[rep_at:rep_at + 1] = [shape[rep_at] // 2, 2]
    names = list(mesh.axis_names)
    names[rep_at:rep_at + 1] = ["x", "core"]
    split = jax.sharding.Mesh(mesh.devices.reshape(shape), tuple(names))
    rows = P(("x", "core", "ctx"), None)
    placed = (rows, rows, rows, P(("x", "core")), P(), P("ctx", None))
    return jax.shard_map(body, mesh=split, in_specs=placed, out_specs=rows, check_vma=False)
```

```python
import functools
import math

import jax
import jax.numpy as jnp
from jax import lax
from jax.experimental import pallas as pl
from jax.experimental.pallas import tpu as pltpu
from jax.sharding import PartitionSpec as P


HEAD_DIM = 128
PHM_N = 4
UNIT = 128
BQ = 512
BK = 256


def flash_kernel(ends_ref, q_ref, k_ref, v_ref, o_ref):
    i = pl.program_id(0)
    e0 = ends_ref[0]
    e1 = ends_ref[1]
    scale = 1.0 / math.sqrt(HEAD_DIM)
    per = BK // UNIT

    def doc_start(t):
        return jnp.where(t >= e1, e1, jnp.where(t >= e0, e0, 0))

    q_lo = i * BQ
    q_hi = q_lo + BQ - 1
    j_lo = doc_start(q_lo) // BK
    j_hi = q_hi // BK
    full_lo = (doc_start(q_hi) + BK - 1) // BK
    full_hi = (q_lo + 1) // BK - 1
    mid_lo = jnp.maximum(j_lo, jnp.minimum(full_lo, j_hi + 1))
    mid_hi = jnp.maximum(mid_lo, full_hi + 1)
    q = q_ref[...].reshape(BQ, HEAD_DIM)
    q_pos = q_lo + lax.broadcasted_iota(jnp.int32, (BQ, 1), 0)
    q_start = doc_start(q_pos)

    def step(j, carry, masked):
        m, l, acc = carry
        k = k_ref[pl.ds(j * per, per)].reshape(BK, HEAD_DIM)
        v = v_ref[pl.ds(j * per, per)].reshape(BK, HEAD_DIM)
        s = lax.dot_general(
            q, k, (((1,), (1,)), ((), ())), preferred_element_type=jnp.float32
        ) * scale
        if masked:
            k_pos = j * BK + lax.broadcasted_iota(jnp.int32, (1, BK), 1)
            mask = k_pos <= q_pos
            if masked == "both":
                mask = mask & (k_pos >= q_start)
            s = jnp.where(mask, s, -jnp.inf)
        m_new = jnp.maximum(m, jnp.max(s, axis=1, keepdims=True))
        p = jnp.exp(s - m_new)
        alpha = jnp.exp(m - m_new)
        l = alpha * l + jnp.sum(p, axis=1, keepdims=True)
        acc = alpha * acc + jnp.dot(
            p.astype(jnp.bfloat16), v, preferred_element_type=jnp.float32
        )
        return m_new, l, acc

    carry = (
        jnp.full((BQ, 1), -1e30, jnp.float32),
        jnp.zeros((BQ, 1), jnp.float32),
        jnp.zeros((BQ, HEAD_DIM), jnp.float32),
    )
    edge = functools.partial(step, masked="both")
    inner = functools.partial(step, masked=None)
    diagonal = functools.partial(step, masked="causal")
    carry = lax.fori_loop(j_lo, mid_lo, edge, carry)
    carry = lax.fori_loop(mid_lo, mid_hi, inner, carry)
    _, l, acc = lax.fori_loop(mid_hi, j_hi + 1, diagonal, carry)
    o_ref[...] = (acc / l).astype(o_ref.dtype)


def attend(qkv, ends):
    blocks = qkv.shape[0]
    seq = blocks * UNIT

    def whole(which):
        return pl.BlockSpec((blocks, None, UNIT, HEAD_DIM), lambda i, e: (0, which, 0, 0))

    return pl.pallas_call(
        flash_kernel,
        grid_spec=pltpu.PrefetchScalarGridSpec(
            num_scalar_prefetch=1,
            grid=(seq // BQ,),
            in_specs=[
                pl.BlockSpec((BQ // UNIT, None, UNIT, HEAD_DIM), lambda i, e: (i, 0, 0, 0)),
                whole(1),
                whole(2),
            ],
            out_specs=pl.BlockSpec((BQ, HEAD_DIM), lambda i, e: (i, 0)),
        ),
        out_shape=jax.ShapeDtypeStruct((seq, HEAD_DIM), jnp.bfloat16),
    )(ends, qkv, qkv, qkv)


def pack_kernel(q_ref, k_ref, v_ref, o_ref):
    for h in range(o_ref.shape[0]):
        for w, x_ref in enumerate((q_ref, k_ref, v_ref)):
            o_ref[h, w] = x_ref[:, h * HEAD_DIM:(h + 1) * HEAD_DIM]


def pack(queries, key_rows, value_rows):
    tok, width = queries.shape
    heads = width // HEAD_DIM
    groups = 2
    per = heads // groups
    spec = pl.BlockSpec((tok, per * HEAD_DIM), lambda g: (0, g))
    return pl.pallas_call(
        pack_kernel,
        grid=(groups,),
        in_specs=[spec, spec, spec],
        out_specs=pl.BlockSpec((per, 3, tok, HEAD_DIM), lambda g: (g, 0, 0, 0)),
        out_shape=jax.ShapeDtypeStruct((heads, 3, tok, HEAD_DIM), queries.dtype),
    )(queries, key_rows, value_rows)


def proj_kernel(mix_ref, att_ref, w_ref, o_ref, acc_ref, mixed_ref, wide_ref):
    i = pl.program_id(0)
    halves, slots, sub, cols = w_ref.shape

    @pl.when(i == 0)
    def _():
        acc_ref[...] = jnp.zeros_like(acc_ref)
        for h in range(att_ref.shape[0]):
            wide_ref[h] = att_ref[h].astype(jnp.float32)

    for b in range(PHM_N):
        for s in range(slots):
            part = wide_ref[s] * mix_ref[(i * PHM_N + 0) * PHM_N + b]
            for a in range(1, PHM_N):
                part = part + wide_ref[a * slots + s] * mix_ref[(i * PHM_N + a) * PHM_N + b]
            part = part.astype(jnp.bfloat16)
            for h in range(halves):
                mixed_ref[h, :, s * sub:(s + 1) * sub] = part[:, h * sub:(h + 1) * sub]
        for h in range(halves):
            acc_ref[b] += jnp.dot(
                mixed_ref[h], w_ref[h].reshape(slots * sub, cols), preferred_element_type=jnp.float32
            )

    @pl.when(i == PHM_N - 1)
    def _():
        for b in range(PHM_N):
            o_ref[:, b * cols:(b + 1) * cols] = acc_ref[b].astype(o_ref.dtype)


def project(att, mix, w):
    heads, tok, _ = att.shape
    halves, shards, sub, cols = w.shape
    slots = shards // PHM_N
    return pl.pallas_call(
        proj_kernel,
        grid=(PHM_N,),
        in_specs=[
            pl.BlockSpec(memory_space=pltpu.SMEM),
            pl.BlockSpec((heads, tok, HEAD_DIM), lambda i: (0, 0, 0)),
            pl.BlockSpec((halves, slots, sub, cols), lambda i: (0, i, 0, 0)),
        ],
        out_specs=pl.BlockSpec((tok, PHM_N * cols), lambda i: (0, 0)),
        out_shape=jax.ShapeDtypeStruct((tok, PHM_N * cols), jnp.bfloat16),
        scratch_shapes=[
            pltpu.VMEM((PHM_N, tok, cols), jnp.float32),
            pltpu.VMEM((halves, tok, slots * sub), jnp.bfloat16),
            pltpu.VMEM((heads, tok, HEAD_DIM), jnp.float32),
        ],
    )(mix.reshape(-1), att, w)


def gather_factors(phm_blocks):
    rows = phm_blocks.shape[0]
    half = rows // lax.axis_size("core")
    mine = lax.dynamic_slice_in_dim(phm_blocks, lax.axis_index("core") * half, half, 0)
    over_ctx = lax.all_gather(mine, "ctx", axis=0)
    return lax.all_gather(over_ctx, "core", axis=0)


def body(queries, key_rows, value_rows, doc_blocks, phm_mix, phm_blocks):
    tok_rows = queries.shape[0]
    heads = queries.shape[1] // HEAD_DIM
    factors = gather_factors(phm_blocks)
    stacked = pack(queries, key_rows, value_rows)
    gathered = lax.all_to_all(stacked, "ctx", split_axis=0, concat_axis=0, tiled=True)
    ends = jnp.cumsum(doc_blocks.astype(jnp.int32) * UNIT).astype(jnp.int32)
    attended = attend(gathered, ends)
    returned = lax.all_to_all(
        attended.reshape(heads, tok_rows, HEAD_DIM), "ctx", split_axis=0, concat_axis=0, tiled=True
    )
    return project(returned, phm_mix, factors)


def solution(mesh):
    rep_at = mesh.axis_names.index("rep")
    shape = list(mesh.devices.shape)
    shape[rep_at:rep_at + 1] = [shape[rep_at] // 2, 2]
    names = list(mesh.axis_names)
    names[rep_at:rep_at + 1] = ["x", "core"]
    split = jax.sharding.Mesh(mesh.devices.reshape(shape), tuple(names))
    rows = P(("x", "core", "ctx"), None)
    placed = (rows, rows, rows, P(("x", "core")), P(), P("ctx", None))
    return jax.shard_map(body, mesh=split, in_specs=placed, out_specs=rows, check_vma=False)
```

```python
import functools
import math

import jax
import jax.numpy as jnp
from jax import lax
from jax.experimental import pallas as pl
from jax.experimental.pallas import tpu as pltpu
from jax.sharding import PartitionSpec as P


HEAD_DIM = 128
PHM_N = 4
UNIT = 128
BQ = 512
BK = 256


def flash_kernel(ends_ref, q_ref, k_ref, v_ref, o_ref):
    i = pl.program_id(0)
    e0 = ends_ref[0]
    e1 = ends_ref[1]
    scale = math.log2(math.e) / math.sqrt(HEAD_DIM)
    per = BK // UNIT

    def doc_start(t):
        return jnp.where(t >= e1, e1, jnp.where(t >= e0, e0, 0))

    q_lo = i * BQ
    q_hi = q_lo + BQ - 1
    j_lo = doc_start(q_lo) // BK
    j_hi = q_hi // BK
    full_lo = (doc_start(q_hi) + BK - 1) // BK
    full_hi = (q_lo + 1) // BK - 1
    mid_lo = jnp.maximum(j_lo, jnp.minimum(full_lo, j_hi + 1))
    mid_hi = jnp.maximum(mid_lo, full_hi + 1)
    q = q_ref[...].reshape(BQ, HEAD_DIM)
    q_pos = q_lo + lax.broadcasted_iota(jnp.int32, (BQ, 1), 0)
    q_start = doc_start(q_pos)

    def step(j, carry, masked):
        m, l, acc = carry
        k = k_ref[pl.ds(j * per, per)].reshape(BK, HEAD_DIM)
        v = v_ref[pl.ds(j * per, per)].reshape(BK, HEAD_DIM)
        s = lax.dot_general(
            q, k, (((1,), (1,)), ((), ())), preferred_element_type=jnp.float32
        ) * scale
        if masked:
            k_pos = j * BK + lax.broadcasted_iota(jnp.int32, (1, BK), 1)
            mask = k_pos <= q_pos
            if masked == "both":
                mask = mask & (k_pos >= q_start)
            s = jnp.where(mask, s, -jnp.inf)
        m_new = jnp.maximum(m, jnp.max(s, axis=1, keepdims=True))
        p = jnp.exp2(s - m_new)
        alpha = jnp.exp2(m - m_new)
        l = alpha * l + jnp.sum(p, axis=1, keepdims=True)
        acc = alpha * acc + jnp.dot(
            p.astype(jnp.bfloat16), v, preferred_element_type=jnp.float32
        )
        return m_new, l, acc

    carry = (
        jnp.full((BQ, 1), -1e30, jnp.float32),
        jnp.zeros((BQ, 1), jnp.float32),
        jnp.zeros((BQ, HEAD_DIM), jnp.float32),
    )
    edge = functools.partial(step, masked="both")
    inner = functools.partial(step, masked=None)
    diagonal = functools.partial(step, masked="causal")
    carry = lax.fori_loop(j_lo, mid_lo, edge, carry)
    carry = lax.fori_loop(mid_lo, mid_hi, inner, carry)
    _, l, acc = lax.fori_loop(mid_hi, j_hi + 1, diagonal, carry)
    o_ref[...] = (acc / l).astype(o_ref.dtype)


def attend(qkv, ends):
    blocks = qkv.shape[0]
    seq = blocks * UNIT

    def whole(which):
        return pl.BlockSpec((blocks, None, UNIT, HEAD_DIM), lambda i, e: (0, which, 0, 0))

    return pl.pallas_call(
        flash_kernel,
        grid_spec=pltpu.PrefetchScalarGridSpec(
            num_scalar_prefetch=1,
            grid=(seq // BQ,),
            in_specs=[
                pl.BlockSpec((BQ // UNIT, None, UNIT, HEAD_DIM), lambda i, e: (i, 0, 0, 0)),
                whole(1),
                whole(2),
            ],
            out_specs=pl.BlockSpec((BQ, HEAD_DIM), lambda i, e: (i, 0)),
        ),
        out_shape=jax.ShapeDtypeStruct((seq, HEAD_DIM), jnp.bfloat16),
    )(ends, qkv, qkv, qkv)


def pack_kernel(q_ref, k_ref, v_ref, o_ref):
    for h in range(o_ref.shape[0]):
        for w, x_ref in enumerate((q_ref, k_ref, v_ref)):
            o_ref[h, w] = x_ref[:, h * HEAD_DIM:(h + 1) * HEAD_DIM]


def pack(queries, key_rows, value_rows):
    tok, width = queries.shape
    heads = width // HEAD_DIM
    groups = 2
    per = heads // groups
    spec = pl.BlockSpec((tok, per * HEAD_DIM), lambda g: (0, g))
    return pl.pallas_call(
        pack_kernel,
        grid=(groups,),
        in_specs=[spec, spec, spec],
        out_specs=pl.BlockSpec((per, 3, tok, HEAD_DIM), lambda g: (g, 0, 0, 0)),
        out_shape=jax.ShapeDtypeStruct((heads, 3, tok, HEAD_DIM), queries.dtype),
    )(queries, key_rows, value_rows)


def proj_kernel(mix_ref, att_ref, w_ref, o_ref, acc_ref, mixed_ref, wide_ref):
    i = pl.program_id(0)
    halves, slots, sub, cols = w_ref.shape

    @pl.when(i == 0)
    def _():
        acc_ref[...] = jnp.zeros_like(acc_ref)
        for h in range(att_ref.shape[0]):
            wide_ref[h] = att_ref[h].astype(jnp.float32)

    for b in range(PHM_N):
        for s in range(slots):
            part = wide_ref[s] * mix_ref[(i * PHM_N + 0) * PHM_N + b]
            for a in range(1, PHM_N):
                part = part + wide_ref[a * slots + s] * mix_ref[(i * PHM_N + a) * PHM_N + b]
            part = part.astype(jnp.bfloat16)
            for h in range(halves):
                mixed_ref[h, :, s * sub:(s + 1) * sub] = part[:, h * sub:(h + 1) * sub]
        for h in range(halves):
            acc_ref[b] += jnp.dot(
                mixed_ref[h], w_ref[h].reshape(slots * sub, cols), preferred_element_type=jnp.float32
            )

    @pl.when(i == PHM_N - 1)
    def _():
        for b in range(PHM_N):
            o_ref[:, b * cols:(b + 1) * cols] = acc_ref[b].astype(o_ref.dtype)


def project(att, mix, w):
    heads, tok, _ = att.shape
    halves, shards, sub, cols = w.shape
    slots = shards // PHM_N
    return pl.pallas_call(
        proj_kernel,
        grid=(PHM_N,),
        in_specs=[
            pl.BlockSpec(memory_space=pltpu.SMEM),
            pl.BlockSpec((heads, tok, HEAD_DIM), lambda i: (0, 0, 0)),
            pl.BlockSpec((halves, slots, sub, cols), lambda i: (0, i, 0, 0)),
        ],
        out_specs=pl.BlockSpec((tok, PHM_N * cols), lambda i: (0, 0)),
        out_shape=jax.ShapeDtypeStruct((tok, PHM_N * cols), jnp.bfloat16),
        scratch_shapes=[
            pltpu.VMEM((PHM_N, tok, cols), jnp.float32),
            pltpu.VMEM((halves, tok, slots * sub), jnp.bfloat16),
            pltpu.VMEM((heads, tok, HEAD_DIM), jnp.float32),
        ],
    )(mix.reshape(-1), att, w)


def gather_factors(phm_blocks):
    rows = phm_blocks.shape[0]
    half = rows // lax.axis_size("core")
    mine = lax.dynamic_slice_in_dim(phm_blocks, lax.axis_index("core") * half, half, 0)
    over_ctx = lax.all_gather(mine, "ctx", axis=0)
    return lax.all_gather(over_ctx, "core", axis=0)


def body(queries, key_rows, value_rows, doc_blocks, phm_mix, phm_blocks):
    tok_rows = queries.shape[0]
    heads = queries.shape[1] // HEAD_DIM
    factors = gather_factors(phm_blocks)
    stacked = pack(queries, key_rows, value_rows)
    gathered = lax.all_to_all(stacked, "ctx", split_axis=0, concat_axis=0, tiled=True)
    ends = jnp.cumsum(doc_blocks.astype(jnp.int32) * UNIT).astype(jnp.int32)
    attended = attend(gathered, ends)
    returned = lax.all_to_all(
        attended.reshape(heads, tok_rows, HEAD_DIM), "ctx", split_axis=0, concat_axis=0, tiled=True
    )
    return project(returned, phm_mix, factors)


def solution(mesh):
    rep_at = mesh.axis_names.index("rep")
    shape = list(mesh.devices.shape)
    shape[rep_at:rep_at + 1] = [shape[rep_at] // 2, 2]
    names = list(mesh.axis_names)
    names[rep_at:rep_at + 1] = ["x", "core"]
    split = jax.sharding.Mesh(mesh.devices.reshape(shape), tuple(names))
    rows = P(("x", "core", "ctx"), None)
    placed = (rows, rows, rows, P(("x", "core")), P(), P("ctx", None))
    return jax.shard_map(body, mesh=split, in_specs=placed, out_specs=rows, check_vma=False)
```
